256 devices in a mesh: dp: 8 (over y_hi, x), seq: 16 (over y_lo, z), segment: 2 (over core).
Axes of the slice: x: 4, y: 4 (y_hi: 2, y_lo: 2; y = y_hi * 2 + y_lo), z: 8, core: 2. Of those that a mesh axis runs over, the one named last changes fastest.
Arguments:
- saved_input: bfloat16 [2, 8, 8192, 256], P('segment', 'dp', 'seq'), may hold values from -6 to 6
- upstream: bfloat16 [8, 8192, 256], P('dp', 'seq'), may hold values from -6 to 6
- clip_lengths: int32 [8, 32], P('dp'), may hold values from 1 to 2048, 8192 in all within a row
- conv_a: bfloat16 [2, 3, 7, 256, 256], P('segment'), may hold values from -0.125 to 0.125
- bias_a: float32 [2, 3, 256], P('segment'), may hold values from -3 to 3
- conv_b: bfloat16 [2, 3, 256, 256], P('segment'), may hold values from -0.375 to 0.375
Outputs:
- section_input_grad: bfloat16 [2, 8, 8192, 256], P('segment', 'dp', 'seq')
- grad_conv_a: float32 [2, 3, 7, 256, 256], P('segment')
- grad_bias_a: float32 [2, 3, 256], P('segment')
- grad_conv_b: float32 [2, 3, 256, 256], P('segment')
The draws below stay inside these ranges and needn't reach their ends.
Inputs may be any that keep to these rules, and one draw needn't show every extreme that they name: `clip_lengths`: each row's 32 lengths sum to 8192, and the longest is exactly 2048.
All inputs are finite; a program needn't handle non-finite values.
Results may differ from the reference program's by a relative error of at most 0.02.
Values may be sent and summed in bfloat16 or wider, within the bound.
No kernel may reach another device: no remote copies, remote signals or barrier semaphores. Data moves between devices by JAX's collectives and lax.ppermute only.
A program may use at most 128 MiB of HBM per device.

```python
import math
import jax
import jax.numpy as jnp
import numpy as np
from jax import lax

CHANNELS = 256
INNER = 256
KERNEL = 7
UNITS = 3
BATCH = 8
TIME = 8192
CLIPS = 32


def levels(key, extent, cuts, smallest, top_value):
    factor_of, own = 1.0, jax.random.fold_in(key, 6)
    for dim, blocks in cuts:
        heights = jnp.exp(jax.random.uniform(jax.random.fold_in(own, dim), (blocks,), jnp.float32, smallest / len(cuts), top_value / len(cuts)))
        factor_of = factor_of * jnp.repeat(heights, extent[dim] // blocks).reshape([-1 if axis == dim else 1 for axis in range(len(extent))])
    return factor_of


def length_profile(count, total, reach, lean):
    loads = [(1 << 20) // math.isqrt(rank ** lean) + 1 for rank in range(2, count + 1)]
    surplus, given = total - reach - (count - 1), [1] * (count - 1)
    while surplus > 0:
        free = [i for i in range(count - 1) if given[i] < reach]
        mass, remaining = sum([loads[i] for i in free]), surplus
        for i in free:
            addition = min(reach - given[i], max(1, remaining * loads[i] // mass), surplus)
            given[i] = given[i] + addition
            surplus = surplus - addition
    return np.array([reach] + given)


def ragged(rng, count, total, reach, slope):
    if count == 2:
        one = jax.random.randint(rng, (), max(1, total - reach), min(reach, total - 1) + 1)
        return jnp.stack([one, total - one])
    sizes = jnp.asarray(length_profile(count, total, reach, slope), jnp.int32)
    twos = (count - 1) // 2
    donor, sink = sizes[1:1 + 2 * twos:2], sizes[2:2 + 2 * twos:2]
    room = jnp.minimum(donor - 1, reach - sink)
    moved = jax.random.randint(jax.random.fold_in(rng, 1), (twos,), 0, 1 << 20) % (room + 1)
    sizes = sizes.at[1:1 + 2 * twos:2].set(donor - moved).at[2:2 + 2 * twos:2].set(sink + moved)
    return sizes[jax.random.permutation(jax.random.fold_in(rng, 2), count)]


def bell_draw(rng, shape, scale, limit, shards=(), kind=jnp.bfloat16):
    values = scale * jax.random.normal(rng, shape, jnp.float32)
    if shards:
        values = values * levels(rng, shape, shards, -0.22, 0.18)
    return jnp.clip(values, -limit, limit).astype(kind)


def setup_inputs(seed: int = 0) -> dict:
    streams_of = jax.random.split(jax.random.key(seed), 7)
    saved_input = bell_draw(streams_of[0], (2, BATCH, TIME, CHANNELS), 1.0, 6.0, ((0, 2), (1, 8), (2, 16)))
    upstream = bell_draw(streams_of[1], (BATCH, TIME, CHANNELS), 1.0, 6.0, ((0, 8), (1, 16)))
    clip_lengths = jax.vmap(lambda own: ragged(own, CLIPS, TIME, TIME // 4, 2))(jax.random.split(streams_of[2], BATCH)).reshape((BATCH, CLIPS)).astype(jnp.int32)
    conv_a = bell_draw(streams_of[3], (2, UNITS, KERNEL, CHANNELS, INNER), (KERNEL * CHANNELS) ** -0.5, 0.125, ((0, 2),))
    bias_a = bell_draw(streams_of[4], (2, UNITS, INNER), 0.5, 3.0, ((0, 2),), jnp.float32)
    conv_b = bell_draw(streams_of[5], (2, UNITS, INNER, CHANNELS), INNER ** -0.5, 0.375, ((0, 2),))
    return dict(saved_input=saved_input, upstream=upstream, clip_lengths=clip_lengths, conv_a=conv_a, bias_a=bias_a, conv_b=conv_b)


def elu_act(value):
    return jnp.where(value > 0, value, jnp.expm1(jnp.minimum(value, 0.0)))


def elu_slope(value):
    return jnp.where(value > 0, 1.0, jnp.exp(jnp.minimum(value, 0.0)))


def shifted(array, shift_by, fill):
    margin = abs(shift_by)
    frames = array.shape[0]
    widths = [(margin, margin)] + [(0, 0)] * (array.ndim - 1)
    padded = jnp.pad(array, widths, constant_values=fill)
    return padded[margin + shift_by:margin + shift_by + frames]


def one_sequence(stream, grad_out, lengths, weights_a, biases_a, weights_b):
    half = KERNEL // 2
    clip_ends = jnp.cumsum(lengths).astype(jnp.int32)
    places = jnp.arange(TIME, dtype=jnp.int32)
    clip_of = jnp.sum((places[:, None] >= clip_ends[None, :]).astype(jnp.int32), axis=1).astype(jnp.int32)
    stored = []
    for unit_idx in range(UNITS):
        dilation = 3 ** unit_idx
        active = elu_act(stream.astype(jnp.float32)).astype(jnp.bfloat16)
        tap_rows = []
        for tap_no in range(KERNEL):
            shift_by = (tap_no - half) * dilation
            within = shifted(clip_of, shift_by, -1) == clip_of
            tap_rows.append(jnp.where(within[:, None], shifted(active, shift_by, 0.0), 0.0).astype(jnp.bfloat16))
        pre_act = biases_a[unit_idx][None, :]
        for tap_no in range(KERNEL):
            pre_act = pre_act + jnp.dot(tap_rows[tap_no], weights_a[unit_idx, tap_no], preferred_element_type=jnp.float32)
        squashed = elu_act(pre_act).astype(jnp.bfloat16)
        next_stream = (stream.astype(jnp.float32) + jnp.dot(squashed, weights_b[unit_idx], preferred_element_type=jnp.float32)).astype(jnp.bfloat16)
        stored.append((stream, tap_rows, pre_act, squashed))
        stream = next_stream
    grad_y = grad_out
    grads_a = [None] * UNITS
    grads_bias = [None] * UNITS
    grads_b = [None] * UNITS
    for unit_idx in reversed(range(UNITS)):
        dilation = 3 ** unit_idx
        stream_in, tap_rows, pre_act, squashed = stored[unit_idx]
        grad_b = jnp.dot(grad_y, weights_b[unit_idx].T, preferred_element_type=jnp.float32)
        gate = (grad_b * elu_slope(pre_act)).astype(jnp.bfloat16)
        grads_b[unit_idx] = jnp.dot(squashed.T, grad_y, preferred_element_type=jnp.float32)
        grads_bias[unit_idx] = jnp.sum(gate.astype(jnp.float32), axis=0)
        grads_a[unit_idx] = jnp.stack([jnp.dot(tap_rows[tap_no].T, gate, preferred_element_type=jnp.float32) for tap_no in range(KERNEL)])
        back = jnp.zeros((TIME, CHANNELS), jnp.float32)
        for tap_no in range(KERNEL):
            shift_by = (tap_no - half) * dilation
            within = shifted(clip_of, -shift_by, -1) == clip_of
            term = jnp.dot(gate, weights_a[unit_idx, tap_no].T, preferred_element_type=jnp.float32)
            back = back + jnp.where(within[:, None], shifted(term, -shift_by, 0.0), 0.0)
        grad_y = (grad_y.astype(jnp.float32) + back * elu_slope(stream_in.astype(jnp.float32))).astype(jnp.bfloat16)
    return grad_y, jnp.stack(grads_a), jnp.stack(grads_bias), jnp.stack(grads_b)


def run_section(segment_no, inputs, grads_out, clip_lengths, conv_a, bias_a, conv_b):
    def runner(item):
        return one_sequence(item[0], item[1], item[2], conv_a[segment_no], bias_a[segment_no], conv_b[segment_no])

    grad_in, part_a, part_bias, part_b = lax.map(runner, (inputs, grads_out, clip_lengths))
    return grad_in, jnp.sum(part_a, axis=0), jnp.sum(part_bias, axis=0), jnp.sum(part_b, axis=0)


def reference(saved_input, upstream, clip_lengths, conv_a, bias_a, conv_b):
    dec_in, dec_a, dec_bias, dec_b = run_section(1, saved_input[1], upstream, clip_lengths, conv_a, bias_a, conv_b)
    enc_in, enc_a, enc_bias, enc_b = run_section(0, saved_input[0], dec_in, clip_lengths, conv_a, bias_a, conv_b)
    return (jnp.stack([enc_in, dec_in]), jnp.stack([enc_a, dec_a]), jnp.stack([enc_bias, dec_bias]), jnp.stack([enc_b, dec_b]))
```

```python
import jax
import jax.numpy as jnp
from jax import lax
from jax.sharding import PartitionSpec as P

KERNEL = 7
UNITS = 3


def with_halo(cells, sides, width):
    for axis, dim in sides:
        count = lax.axis_size(axis)
        ends = count - 1
        head = lax.slice_in_dim(cells, 0, width, axis=dim)
        tail = lax.slice_in_dim(cells, cells.shape[dim] - width, cells.shape[dim], axis=dim)
        cells = jnp.concatenate(
            [
                lax.ppermute(tail, axis, [(i, (i + 1) % count) for i in range(ends)]),
                cells,
                lax.ppermute(head, axis, [((i + 1) % count, i) for i in range(ends)]),
            ],
            axis=dim,
        )
    return cells


def spread(value, axis, root):
    mine = lax.axis_index(axis) == root
    return lax.psum(jnp.where(mine, value, jnp.zeros_like(value)), axis)


def elu_act(value):
    return jnp.where(value > 0, value, jnp.expm1(jnp.minimum(value, 0.0)))


def elu_slope(value):
    return jnp.where(value > 0, 1.0, jnp.exp(jnp.minimum(value, 0.0)))


def spread_acts(active, reach):
    return with_halo(active, (("seq", 0),), reach)


def spread_grads(gate, reach):
    return with_halo(gate, (("seq", 0),), reach)


def shards(saved_input, upstream, clip_lengths, conv_a, bias_a, conv_b):
    stream = saved_input[0, 0]
    lengths = clip_lengths[0]
    weights_a = conv_a[0]
    biases_a = bias_a[0]
    weights_b = conv_b[0]
    frames = stream.shape[0]
    channels = stream.shape[1]
    inner = weights_a.shape[3]
    half = KERNEL // 2
    furthest = half * 3 ** (UNITS - 1)
    offset = lax.axis_index("seq") * frames
    is_decoder = lax.axis_index("segment") == 1
    clip_ends = jnp.cumsum(lengths)
    places = offset - furthest + jnp.arange(frames + 2 * furthest, dtype=jnp.int32)
    clip_of = jnp.sum((places[:, None] >= clip_ends[None, :]).astype(jnp.int32), axis=1)
    own_clip = clip_of[furthest : furthest + frames]

    def linked(shift_by):
        return (clip_of[furthest + shift_by : furthest + shift_by + frames] == own_clip)[:, None]

    stored = []
    for unit_idx in range(UNITS):
        dilation = 3**unit_idx
        reach = half * dilation
        active = elu_act(stream.astype(jnp.float32)).astype(jnp.bfloat16)
        padded = spread_acts(active, reach)
        tap_rows = jnp.concatenate(
            [
                jnp.where(
                    linked((tap_no - half) * dilation),
                    padded[
                        reach
                        + (tap_no - half) * dilation : reach
                        + (tap_no - half) * dilation
                        + frames
                    ],
                    jnp.zeros((), jnp.bfloat16),
                )
                for tap_no in range(KERNEL)
            ],
            axis=1,
        )
        pre_act = biases_a[unit_idx][None, :] + jnp.dot(
            tap_rows,
            weights_a[unit_idx].reshape(KERNEL * channels, inner),
            preferred_element_type=jnp.float32,
        )
        squashed = elu_act(pre_act).astype(jnp.bfloat16)
        next_stream = (
            stream.astype(jnp.float32)
            + jnp.dot(squashed, weights_b[unit_idx], preferred_element_type=jnp.float32)
        ).astype(jnp.bfloat16)
        stored.append((stream, tap_rows, pre_act, squashed))
        stream = next_stream

    def unit_back(unit_idx, grad_y):
        dilation = 3**unit_idx
        reach = half * dilation
        stream_in, tap_rows, pre_act, squashed = stored[unit_idx]
        grad_b = lax.dot_general(
            grad_y,
            weights_b[unit_idx],
            (((1,), (1,)), ((), ())),
            preferred_element_type=jnp.float32,
        )
        gate = (grad_b * elu_slope(pre_act)).astype(jnp.bfloat16)
        gate_padded = spread_grads(gate, reach)
        back_rows = jnp.concatenate(
            [
                jnp.where(
                    linked(-(tap_no - half) * dilation),
                    gate_padded[
                        reach
                        - (tap_no - half) * dilation : reach
                        - (tap_no - half) * dilation
                        + frames
                    ],
                    jnp.zeros((), jnp.bfloat16),
                )
                for tap_no in range(KERNEL)
            ],
            axis=1,
        )
        turned = jnp.transpose(weights_a[unit_idx], (0, 2, 1)).reshape(KERNEL * inner, channels)
        back = jnp.dot(back_rows, turned, preferred_element_type=jnp.float32)
        grad_next = (
            grad_y.astype(jnp.float32) + back * elu_slope(stream_in.astype(jnp.float32))
        ).astype(jnp.bfloat16)
        return (gate, grad_next)

    first_gates = [None] * UNITS
    first_grads = [None] * (UNITS + 1)
    grad_y = upstream[0]
    first_grads[UNITS] = grad_y
    for unit_idx in reversed(range(UNITS)):
        gate, grad_y = unit_back(unit_idx, grad_y)
        first_gates[unit_idx] = gate
        first_grads[unit_idx] = grad_y
    latent = lax.ppermute(grad_y, "segment", [(1, 0)])
    grads_a = [None] * UNITS
    grads_bias = [None] * UNITS
    grads_b = [None] * UNITS
    contract = (((0,), (0,)), ((), ()))
    grad_y = latent
    for unit_idx in reversed(range(UNITS)):
        stream_in, tap_rows, pre_act, squashed = stored[unit_idx]
        gate_two, grad_next = unit_back(unit_idx, grad_y)
        gate = jnp.where(is_decoder, first_gates[unit_idx], gate_two)
        grad_out = jnp.where(is_decoder, first_grads[unit_idx + 1], grad_y)
        unit_b = lax.dot_general(squashed, grad_out, contract, preferred_element_type=jnp.float32)
        unit_bias = jnp.sum(gate.astype(jnp.float32), axis=0)
        unit_a = lax.dot_general(
            tap_rows, gate, contract, preferred_element_type=jnp.float32
        ).reshape(KERNEL, channels, inner)
        grads_a[unit_idx] = unit_a
        grads_bias[unit_idx] = unit_bias
        grads_b[unit_idx] = unit_b
        grad_y = grad_next
    section_grad = jnp.where(is_decoder, first_grads[0], grad_y)
    rows_a = UNITS * KERNEL * channels
    rows_b = UNITS * inner
    packed = jnp.concatenate(
        [
            jnp.stack(grads_a).reshape(rows_a, inner),
            jnp.stack(grads_b).reshape(rows_b, channels),
            jnp.pad(jnp.stack(grads_bias), ((0, 8 - UNITS), (0, 0))),
        ],
        axis=0,
    )
    packed = lax.psum(packed, ("dp", "seq"))
    total_a = packed[:rows_a].reshape(UNITS, KERNEL, channels, inner)
    total_b = packed[rows_a : rows_a + rows_b].reshape(UNITS, inner, channels)
    total_bias = packed[rows_a + rows_b : rows_a + rows_b + UNITS]
    return (section_grad[None, None], total_a[None], total_bias[None], total_b[None])


def solution(mesh):
    placed = (
        P("segment", "dp", "seq", None),
        P("dp", "seq", None),
        P("dp", None),
        P("segment", None, None, None, None),
        P("segment", None, None),
        P("segment", None, None, None),
    )
    return jax.shard_map(
        shards,
        mesh=mesh,
        in_specs=placed,
        out_specs=(
            P("segment", "dp", "seq", None),
            P("segment", None, None, None, None),
            P("segment", None, None),
            P("segment", None, None, None),
        ),
        check_vma=False,
    )
```

```python
import jax
import jax.numpy as jnp
from jax import lax
from jax.sharding import PartitionSpec as P

KERNEL = 7
UNITS = 3


def with_halo(cells, sides, width):
    for axis, dim in sides:
        count = lax.axis_size(axis)
        ends = count - 1
        head = lax.slice_in_dim(cells, 0, width, axis=dim)
        tail = lax.slice_in_dim(cells, cells.shape[dim] - width, cells.shape[dim], axis=dim)
        cells = jnp.concatenate(
            [
                lax.ppermute(tail, axis, [(i, (i + 1) % count) for i in range(ends)]),
                cells,
                lax.ppermute(head, axis, [((i + 1) % count, i) for i in range(ends)]),
            ],
            axis=dim,
        )
    return cells


def spread(value, axis, root):
    mine = lax.axis_index(axis) == root
    return lax.psum(jnp.where(mine, value, jnp.zeros_like(value)), axis)


def elu_act(value):
    return jnp.where(value > 0, value, jnp.expm1(jnp.minimum(value, 0.0)))


def elu_slope(value):
    return jnp.where(value > 0, 1.0, jnp.exp(jnp.minimum(value, 0.0)))


def spread_acts(active, reach):
    return with_halo(active, (("seq", 0),), reach)


def spread_grads(gate, reach):
    return with_halo(gate, (("seq", 0),), reach)


def shards(saved_input, upstream, clip_lengths, conv_a, bias_a, conv_b):
    stream = saved_input[0, 0]
    lengths = clip_lengths[0]
    weights_a = conv_a[0]
    biases_a = bias_a[0]
    weights_b = conv_b[0]
    frames = stream.shape[0]
    channels = stream.shape[1]
    inner = weights_a.shape[3]
    half = KERNEL // 2
    furthest = half * 3 ** (UNITS - 1)
    offset = lax.axis_index("seq") * frames
    is_decoder = lax.axis_index("segment") == 1
    clip_ends = jnp.cumsum(lengths)
    places = offset - furthest + jnp.arange(frames + 2 * furthest, dtype=jnp.int32)
    clip_of = jnp.sum((places[:, None] >= clip_ends[None, :]).astype(jnp.int32), axis=1)
    own_clip = clip_of[furthest : furthest + frames]

    def linked(shift_by):
        return (clip_of[furthest + shift_by : furthest + shift_by + frames] == own_clip)[:, None]

    stored = []
    for unit_idx in range(UNITS):
        dilation = 3**unit_idx
        reach = half * dilation
        active = elu_act(stream.astype(jnp.float32)).astype(jnp.bfloat16)
        padded = spread_acts(active, reach)
        tap_rows = jnp.concatenate(
            [
                jnp.where(
                    linked((tap_no - half) * dilation),
                    padded[
                        reach
                        + (tap_no - half) * dilation : reach
                        + (tap_no - half) * dilation
                        + frames
                    ],
                    jnp.zeros((), jnp.bfloat16),
                )
                for tap_no in range(KERNEL)
            ],
            axis=1,
        )
        pre_act = biases_a[unit_idx][None, :] + jnp.dot(
            tap_rows,
            weights_a[unit_idx].reshape(KERNEL * channels, inner),
            preferred_element_type=jnp.float32,
        )
        squashed = elu_act(pre_act).astype(jnp.bfloat16)
        next_stream = (
            stream.astype(jnp.float32)
            + jnp.dot(squashed, weights_b[unit_idx], preferred_element_type=jnp.float32)
        ).astype(jnp.bfloat16)
        stored.append((stream, tap_rows, pre_act, squashed))
        stream = next_stream

    def unit_back(unit_idx, grad_y):
        dilation = 3**unit_idx
        reach = half * dilation
        stream_in, tap_rows, pre_act, squashed = stored[unit_idx]
        grad_b = lax.dot_general(
            grad_y,
            weights_b[unit_idx],
            (((1,), (1,)), ((), ())),
            preferred_element_type=jnp.float32,
        )
        gate = (grad_b * elu_slope(pre_act)).astype(jnp.bfloat16)
        gate_padded = spread_grads(gate, reach)
        back_rows = jnp.concatenate(
            [
                jnp.where(
                    linked(-(tap_no - half) * dilation),
                    gate_padded[
                        reach
                        - (tap_no - half) * dilation : reach
                        - (tap_no - half) * dilation
                        + frames
                    ],
                    jnp.zeros((), jnp.bfloat16),
                )
                for tap_no in range(KERNEL)
            ],
            axis=1,
        )
        turned = jnp.transpose(weights_a[unit_idx], (0, 2, 1)).reshape(KERNEL * inner, channels)
        back = jnp.dot(back_rows, turned, preferred_element_type=jnp.float32)
        grad_next = (
            grad_y.astype(jnp.float32) + back * elu_slope(stream_in.astype(jnp.float32))
        ).astype(jnp.bfloat16)
        return (gate, grad_next)

    first_gates = [None] * UNITS
    first_grads = [None] * (UNITS + 1)
    grad_y = upstream[0]
    first_grads[UNITS] = grad_y
    for unit_idx in reversed(range(UNITS)):
        gate, grad_y = unit_back(unit_idx, grad_y)
        first_gates[unit_idx] = gate
        first_grads[unit_idx] = grad_y
    latent = lax.ppermute(grad_y, "segment", [(1, 0)])
    grads_a = [None] * UNITS
    grads_bias = [None] * UNITS
    grads_b = [None] * UNITS
    contract = (((0,), (0,)), ((), ()))
    grad_y = latent
    for unit_idx in reversed(range(UNITS)):
        stream_in, tap_rows, pre_act, squashed = stored[unit_idx]
        gate_two, grad_next = unit_back(unit_idx, grad_y)
        gate = jnp.where(is_decoder, first_gates[unit_idx], gate_two)
        grad_out = jnp.where(is_decoder, first_grads[unit_idx + 1], grad_y)
        unit_b = lax.dot_general(squashed, grad_out, contract, preferred_element_type=jnp.float32)
        unit_bias = jnp.sum(gate.astype(jnp.float32), axis=0)
        unit_a = lax.dot_general(
            tap_rows, gate, contract, preferred_element_type=jnp.float32
        ).reshape(KERNEL, channels, inner)
        grads_a[unit_idx] = unit_a
        grads_bias[unit_idx] = unit_bias
        grads_b[unit_idx] = unit_b
        grad_y = grad_next
    section_grad = jnp.where(is_decoder, first_grads[0], grad_y)
    rows_a = UNITS * KERNEL * channels
    rows_b = UNITS * inner
    packed = jnp.concatenate(
        [
            jnp.stack(grads_a).reshape(rows_a, inner),
            jnp.stack(grads_b).reshape(rows_b, channels),
            jnp.pad(jnp.stack(grads_bias), ((0, 8 - UNITS), (0, 0))),
        ],
        axis=0,
    )
    group = lax.axis_size("dp") * lax.axis_size("seq")
    rows = packed.shape[0]
    share = -(-rows // (group * 8)) * 8
    packed = jnp.pad(packed, ((0, share * group - rows), (0, 0)))
    packed = lax.psum_scatter(packed, ("dp", "seq"), scatter_dimension=0, tiled=True)
    packed = lax.all_gather(
        packed.astype(jnp.bfloat16), ("dp", "seq"), axis=0, tiled=True
    ).astype(jnp.float32)
    total_a = packed[:rows_a].reshape(UNITS, KERNEL, channels, inner)
    total_b = packed[rows_a : rows_a + rows_b].reshape(UNITS, inner, channels)
    total_bias = packed[rows_a + rows_b : rows_a + rows_b + UNITS]
    return (section_grad[None, None], total_a[None], total_bias[None], total_b[None])


def solution(mesh):
    placed = (
        P("segment", "dp", "seq", None),
        P("dp", "seq", None),
        P("dp", None),
        P("segment", None, None, None, None),
        P("segment", None, None),
        P("segment", None, None, None),
    )
    return jax.shard_map(
        shards,
        mesh=mesh,
        in_specs=placed,
        out_specs=(
            P("segment", "dp", "seq", None),
            P("segment", None, None, None, None),
            P("segment", None, None),
            P("segment", None, None, None),
        ),
        check_vma=False,
    )
```

```python
import jax
import jax.numpy as jnp
from jax import lax
from jax.sharding import PartitionSpec as P

KERNEL = 7
UNITS = 3


def with_halo(cells, sides, width):
    for axis, dim in sides:
        count = lax.axis_size(axis)
        ends = count - 1
        head = lax.slice_in_dim(cells, 0, width, axis=dim)
        tail = lax.slice_in_dim(cells, cells.shape[dim] - width, cells.shape[dim], axis=dim)
        cells = jnp.concatenate(
            [
                lax.ppermute(tail, axis, [(i, (i + 1) % count) for i in range(ends)]),
                cells,
                lax.ppermute(head, axis, [((i + 1) % count, i) for i in range(ends)]),
            ],
            axis=dim,
        )
    return cells


def spread(value, axis, root):
    mine = lax.axis_index(axis) == root
    return lax.psum(jnp.where(mine, value, jnp.zeros_like(value)), axis)


def elu_act(value):
    return jnp.where(value > 0, value, jnp.expm1(jnp.minimum(value, 0.0)))


def elu_slope(value):
    return jnp.where(value > 0, 1.0, jnp.exp(jnp.minimum(value, 0.0)))


def spread_acts(active, reach):
    return with_halo(active, (("seq", 0),), reach)


def spread_grads(gate, reach):
    return with_halo(gate, (("seq", 0),), reach)


def shards(saved_input, upstream, clip_lengths, conv_a, bias_a, conv_b):
    stream = saved_input[0, 0]
    lengths = clip_lengths[0]
    weights_a = conv_a[0]
    biases_a = bias_a[0]
    weights_b = conv_b[0]
    frames = stream.shape[0]
    channels = stream.shape[1]
    inner = weights_a.shape[3]
    half = KERNEL // 2
    furthest = half * 3 ** (UNITS - 1)
    offset = lax.axis_index("seq") * frames
    is_decoder = lax.axis_index("segment") == 1
    clip_ends = jnp.cumsum(lengths)
    places = offset - furthest + jnp.arange(frames + 2 * furthest, dtype=jnp.int32)
    clip_of = jnp.sum((places[:, None] >= clip_ends[None, :]).astype(jnp.int32), axis=1)
    own_clip = clip_of[furthest : furthest + frames]

    def linked(shift_by):
        return (clip_of[furthest + shift_by : furthest + shift_by + frames] == own_clip)[:, None]

    stored = []
    for unit_idx in range(UNITS):
        dilation = 3**unit_idx
        reach = half * dilation
        active = elu_act(stream.astype(jnp.float32)).astype(jnp.bfloat16)
        padded = spread_acts(active, reach)
        tap_rows = jnp.concatenate(
            [
                jnp.where(
                    linked((tap_no - half) * dilation),
                    padded[
                        reach
                        + (tap_no - half) * dilation : reach
                        + (tap_no - half) * dilation
                        + frames
                    ],
                    jnp.zeros((), jnp.bfloat16),
                )
                for tap_no in range(KERNEL)
            ],
            axis=1,
        )
        pre_act = biases_a[unit_idx][None, :] + jnp.dot(
            tap_rows,
            weights_a[unit_idx].reshape(KERNEL * channels, inner),
            preferred_element_type=jnp.float32,
        )
        squashed = elu_act(pre_act).astype(jnp.bfloat16)
        next_stream = (
            stream.astype(jnp.float32)
            + jnp.dot(squashed, weights_b[unit_idx], preferred_element_type=jnp.float32)
        ).astype(jnp.bfloat16)
        stored.append((stream, tap_rows, pre_act, squashed))
        stream = next_stream

    def unit_back(unit_idx, grad_y):
        dilation = 3**unit_idx
        reach = half * dilation
        stream_in, tap_rows, pre_act, squashed = stored[unit_idx]
        grad_b = lax.dot_general(
            grad_y,
            weights_b[unit_idx],
            (((1,), (1,)), ((), ())),
            preferred_element_type=jnp.float32,
        )
        gate = (grad_b * elu_slope(pre_act)).astype(jnp.bfloat16)
        gate_padded = spread_grads(gate, reach)
        back_rows = jnp.concatenate(
            [
                jnp.where(
                    linked(-(tap_no - half) * dilation),
                    gate_padded[
                        reach
                        - (tap_no - half) * dilation : reach
                        - (tap_no - half) * dilation
                        + frames
                    ],
                    jnp.zeros((), jnp.bfloat16),
                )
                for tap_no in range(KERNEL)
            ],
            axis=1,
        )
        turned = jnp.transpose(weights_a[unit_idx], (0, 2, 1)).reshape(KERNEL * inner, channels)
        back = jnp.dot(back_rows, turned, preferred_element_type=jnp.float32)
        grad_next = (
            grad_y.astype(jnp.float32) + back * elu_slope(stream_in.astype(jnp.float32))
        ).astype(jnp.bfloat16)
        return (gate, grad_next)

    first_gates = [None] * UNITS
    first_grads = [None] * (UNITS + 1)
    grad_y = upstream[0]
    first_grads[UNITS] = grad_y
    for unit_idx in reversed(range(UNITS)):
        gate, grad_y = unit_back(unit_idx, grad_y)
        first_gates[unit_idx] = gate
        first_grads[unit_idx] = grad_y
    latent = lax.ppermute(grad_y, "segment", [(1, 0)])
    grads_a = [None] * UNITS
    grads_bias = [None] * UNITS
    grads_b = [None] * UNITS
    contract = (((0,), (0,)), ((), ()))
    grad_y = latent
    for unit_idx in reversed(range(UNITS)):
        stream_in, tap_rows, pre_act, squashed = stored[unit_idx]
        gate_two, grad_next = unit_back(unit_idx, grad_y)
        gate = jnp.where(is_decoder, first_gates[unit_idx], gate_two)
        grad_out = jnp.where(is_decoder, first_grads[unit_idx + 1], grad_y)
        unit_b = lax.dot_general(squashed, grad_out, contract, preferred_element_type=jnp.float32)
        unit_bias = jnp.sum(gate.astype(jnp.float32), axis=0)
        unit_a = lax.dot_general(
            tap_rows, gate, contract, preferred_element_type=jnp.float32
        ).reshape(KERNEL, channels, inner)
        grads_a[unit_idx] = unit_a
        grads_bias[unit_idx] = unit_bias
        grads_b[unit_idx] = unit_b
        grad_y = grad_next
    section_grad = jnp.where(is_decoder, first_grads[0], grad_y)
    rows_a = UNITS * KERNEL * channels
    rows_b = UNITS * inner
    packed = jnp.concatenate(
        [
            jnp.stack(grads_a).reshape(rows_a, inner),
            jnp.stack(grads_b).reshape(rows_b, channels),
            jnp.pad(jnp.stack(grads_bias), ((0, 8 - UNITS), (0, 0))),
        ],
        axis=0,
    )
    packed = lax.psum(packed.astype(jnp.bfloat16), ("dp", "seq")).astype(jnp.float32)
    total_a = packed[:rows_a].reshape(UNITS, KERNEL, channels, inner)
    total_b = packed[rows_a : rows_a + rows_b].reshape(UNITS, inner, channels)
    total_bias = packed[rows_a + rows_b : rows_a + rows_b + UNITS]
    return (section_grad[None, None], total_a[None], total_bias[None], total_b[None])


def solution(mesh):
    placed = (
        P("segment", "dp", "seq", None),
        P("dp", "seq", None),
        P("dp", None),
        P("segment", None, None, None, None),
        P("segment", None, None),
        P("segment", None, None, None),
    )
    return jax.shard_map(
        shards,
        mesh=mesh,
        in_specs=placed,
        out_specs=(
            P("segment", "dp", "seq", None),
            P("segment", None, None, None, None),
            P("segment", None, None),
            P("segment", None, None, None),
        ),
        check_vma=False,
    )
```

```python
import jax
import jax.numpy as jnp
from jax import lax
from jax.sharding import PartitionSpec as P

KERNEL = 7
UNITS = 3


def with_halo(cells, sides, width):
    for axis, dim in sides:
        count = lax.axis_size(axis)
        ends = count - 1
        head = lax.slice_in_dim(cells, 0, width, axis=dim)
        tail = lax.slice_in_dim(cells, cells.shape[dim] - width, cells.shape[dim], axis=dim)
        cells = jnp.concatenate(
            [
                lax.ppermute(tail, axis, [(i, (i + 1) % count) for i in range(ends)]),
                cells,
                lax.ppermute(head, axis, [((i + 1) % count, i) for i in range(ends)]),
            ],
            axis=dim,
        )
    return cells


def spread(value, axis, root):
    mine = lax.axis_index(axis) == root
    return lax.psum(jnp.where(mine, value, jnp.zeros_like(value)), axis)


def elu_act(value):
    return jnp.where(value > 0, value, jnp.expm1(jnp.minimum(value, 0.0)))


def elu_slope(value):
    return jnp.where(value > 0, 1.0, jnp.exp(jnp.minimum(value, 0.0)))


def spread_acts(active, reach):
    return with_halo(active, (("seq", 0),), reach)


def spread_grads(gate, reach):
    return with_halo(gate, (("seq", 0),), reach)


def shards(saved_input, upstream, clip_lengths, conv_a, bias_a, conv_b):
    lengths = clip_lengths[0]
    weights_a = conv_a[0]
    biases_a = bias_a[0]
    weights_b = conv_b[0]
    frames = saved_input.shape[2]
    channels = saved_input.shape[3]
    inner = weights_a.shape[3]
    half = KERNEL // 2
    reaches = [half * 3**unit_idx for unit_idx in range(UNITS)]
    margin = 3 * sum(reaches)
    span = frames + 2 * margin
    total = frames * lax.axis_size("seq")
    offset = lax.axis_index("seq") * frames
    is_decoder = lax.axis_index("segment") == 1
    clip_ends = jnp.cumsum(lengths)
    places = offset - margin + jnp.arange(span, dtype=jnp.int32)
    clip_of = jnp.sum((places[:, None] >= clip_ends[None, :]).astype(jnp.int32), axis=1)
    clip_of = jnp.where(places < 0, -1, clip_of)
    clip_of = jnp.where(places >= total, lengths.shape[0], clip_of)
    own = slice(margin, margin + frames)

    def linked(shift_by):
        edge = abs(shift_by)
        padded_ids = jnp.pad(clip_of, (edge, edge), constant_values=-2)
        return (padded_ids[edge + shift_by : edge + shift_by + span] == clip_of)[:, None]

    def shifted_rows(values, shift_by):
        edge = abs(shift_by)
        padded = jnp.pad(values, ((edge, edge), (0, 0)))
        return jnp.where(
            linked(shift_by),
            padded[edge + shift_by : edge + shift_by + span],
            jnp.zeros((), values.dtype),
        )

    stream = with_halo(saved_input[0, 0], (("seq", 0),), margin)
    grad_top = with_halo(upstream[0], (("seq", 0),), margin)

    stored = []
    for unit_idx in range(UNITS):
        dilation = 3**unit_idx
        active = elu_act(stream.astype(jnp.float32)).astype(jnp.bfloat16)
        tap_rows = jnp.concatenate(
            [shifted_rows(active, (tap_no - half) * dilation) for tap_no in range(KERNEL)],
            axis=1,
        )
        pre_act = biases_a[unit_idx][None, :] + jnp.dot(
            tap_rows,
            weights_a[unit_idx].reshape(KERNEL * channels, inner),
            preferred_element_type=jnp.float32,
        )
        squashed = elu_act(pre_act).astype(jnp.bfloat16)
        next_stream = (
            stream.astype(jnp.float32)
            + jnp.dot(squashed, weights_b[unit_idx], preferred_element_type=jnp.float32)
        ).astype(jnp.bfloat16)
        stored.append((stream, tap_rows, pre_act, squashed))
        stream = next_stream

    def unit_back(unit_idx, grad_y):
        dilation = 3**unit_idx
        stream_in, tap_rows, pre_act, squashed = stored[unit_idx]
        grad_b = lax.dot_general(
            grad_y,
            weights_b[unit_idx],
            (((1,), (1,)), ((), ())),
            preferred_element_type=jnp.float32,
        )
        gate = (grad_b * elu_slope(pre_act)).astype(jnp.bfloat16)
        back_rows = jnp.concatenate(
            [shifted_rows(gate, -(tap_no - half) * dilation) for tap_no in range(KERNEL)],
            axis=1,
        )
        turned = jnp.transpose(weights_a[unit_idx], (0, 2, 1)).reshape(KERNEL * inner, channels)
        back = jnp.dot(back_rows, turned, preferred_element_type=jnp.float32)
        grad_next = (
            grad_y.astype(jnp.float32) + back * elu_slope(stream_in.astype(jnp.float32))
        ).astype(jnp.bfloat16)
        return (gate, grad_next)

    first_gates = [None] * UNITS
    first_grads = [None] * (UNITS + 1)
    grad_y = grad_top
    first_grads[UNITS] = grad_y
    for unit_idx in reversed(range(UNITS)):
        gate, grad_y = unit_back(unit_idx, grad_y)
        first_gates[unit_idx] = gate
        first_grads[unit_idx] = grad_y
    latent = lax.ppermute(grad_y, "segment", [(1, 0)])
    grads_a = [None] * UNITS
    grads_bias = [None] * UNITS
    grads_b = [None] * UNITS
    contract = (((0,), (0,)), ((), ()))
    grad_y = latent
    for unit_idx in reversed(range(UNITS)):
        stream_in, tap_rows, pre_act, squashed = stored[unit_idx]
        gate_two, grad_next = unit_back(unit_idx, grad_y)
        gate = jnp.where(is_decoder, first_gates[unit_idx][own], gate_two[own])
        grad_out = jnp.where(is_decoder, first_grads[unit_idx + 1][own], grad_y[own])
        unit_b = lax.dot_general(
            squashed[own], grad_out, contract, preferred_element_type=jnp.float32
        )
        unit_bias = jnp.sum(gate.astype(jnp.float32), axis=0)
        unit_a = lax.dot_general(
            tap_rows[own], gate, contract, preferred_element_type=jnp.float32
        ).reshape(KERNEL, channels, inner)
        grads_a[unit_idx] = unit_a
        grads_bias[unit_idx] = unit_bias
        grads_b[unit_idx] = unit_b
        grad_y = grad_next
    section_grad = jnp.where(is_decoder, first_grads[0][own], grad_y[own])
    rows_a = UNITS * KERNEL * channels
    rows_b = UNITS * inner
    packed = jnp.concatenate(
        [
            jnp.stack(grads_a).reshape(rows_a, inner),
            jnp.stack(grads_b).reshape(rows_b, channels),
            jnp.pad(jnp.stack(grads_bias), ((0, 8 - UNITS), (0, 0))),
        ],
        axis=0,
    )
    packed = lax.psum(packed, ("dp", "seq"))
    total_a = packed[:rows_a].reshape(UNITS, KERNEL, channels, inner)
    total_b = packed[rows_a : rows_a + rows_b].reshape(UNITS, inner, channels)
    total_bias = packed[rows_a + rows_b : rows_a + rows_b + UNITS]
    return (section_grad[None, None], total_a[None], total_bias[None], total_b[None])


def solution(mesh):
    placed = (
        P("segment", "dp", "seq", None),
        P("dp", "seq", None),
        P("dp", None),
        P("segment", None, None, None, None),
        P("segment", None, None),
        P("segment", None, None, None),
    )
    return jax.shard_map(
        shards,
        mesh=mesh,
        in_specs=placed,
        out_specs=(
            P("segment", "dp", "seq", None),
            P("segment", None, None, None, None),
            P("segment", None, None),
            P("segment", None, None, None),
        ),
        check_vma=False,
    )
```

```python
import jax
import jax.numpy as jnp
from jax import lax
from jax.sharding import PartitionSpec as P

KERNEL = 7
UNITS = 3


def with_halo(cells, sides, width):
    for axis, dim in sides:
        count = lax.axis_size(axis)
        ends = count - 1
        head = lax.slice_in_dim(cells, 0, width, axis=dim)
        tail = lax.slice_in_dim(cells, cells.shape[dim] - width, cells.shape[dim], axis=dim)
        cells = jnp.concatenate(
            [
                lax.ppermute(tail, axis, [(i, (i + 1) % count) for i in range(ends)]),
                cells,
                lax.ppermute(head, axis, [((i + 1) % count, i) for i in range(ends)]),
            ],
            axis=dim,
        )
    return cells


def spread(value, axis, root):
    mine = lax.axis_index(axis) == root
    return lax.psum(jnp.where(mine, value, jnp.zeros_like(value)), axis)


def elu_act(value):
    return jnp.where(value > 0, value, jnp.expm1(jnp.minimum(value, 0.0)))


def elu_slope(value):
    return jnp.where(value > 0, 1.0, jnp.exp(jnp.minimum(value, 0.0)))


def spread_acts(active, reach):
    return with_halo(active, (("seq", 0),), reach)


def spread_grads(gate, reach):
    return with_halo(gate, (("seq", 0),), reach)


def shards(saved_input, upstream, clip_lengths, conv_a, bias_a, conv_b):
    lengths = clip_lengths[0]
    weights_a = conv_a[0]
    biases_a = bias_a[0]
    weights_b = conv_b[0]
    frames = saved_input.shape[2]
    channels = saved_input.shape[3]
    inner = weights_a.shape[3]
    half = KERNEL // 2
    reaches = [half * 3**unit_idx for unit_idx in range(UNITS)]
    margin = 3 * sum(reaches)
    span = frames + 2 * margin
    total = frames * lax.axis_size("seq")
    offset = lax.axis_index("seq") * frames
    is_decoder = lax.axis_index("segment") == 1
    clip_ends = jnp.cumsum(lengths)
    places = offset - margin + jnp.arange(span, dtype=jnp.int32)
    clip_of = jnp.sum((places[:, None] >= clip_ends[None, :]).astype(jnp.int32), axis=1)
    clip_of = jnp.where(places < 0, -1, clip_of)
    clip_of = jnp.where(places >= total, lengths.shape[0], clip_of)
    own = slice(margin, margin + frames)

    def linked(shift_by):
        edge = abs(shift_by)
        padded_ids = jnp.pad(clip_of, (edge, edge), constant_values=-2)
        return (padded_ids[edge + shift_by : edge + shift_by + span] == clip_of)[:, None]

    def shifted_rows(values, shift_by):
        edge = abs(shift_by)
        padded = jnp.pad(values, ((edge, edge), (0, 0)))
        return jnp.where(
            linked(shift_by),
            padded[edge + shift_by : edge + shift_by + span],
            jnp.zeros((), values.dtype),
        )

    both = with_halo(
        jnp.concatenate([saved_input[0, 0], upstream[0]], axis=1), (("seq", 0),), margin
    )
    stream = both[:, :channels]
    grad_top = both[:, channels:]

    stored = []
    for unit_idx in range(UNITS):
        dilation = 3**unit_idx
        active = elu_act(stream.astype(jnp.float32)).astype(jnp.bfloat16)
        tap_rows = jnp.concatenate(
            [shifted_rows(active, (tap_no - half) * dilation) for tap_no in range(KERNEL)],
            axis=1,
        )
        pre_act = biases_a[unit_idx][None, :] + jnp.dot(
            tap_rows,
            weights_a[unit_idx].reshape(KERNEL * channels, inner),
            preferred_element_type=jnp.float32,
        )
        squashed = elu_act(pre_act).astype(jnp.bfloat16)
        next_stream = (
            stream.astype(jnp.float32)
            + jnp.dot(squashed, weights_b[unit_idx], preferred_element_type=jnp.float32)
        ).astype(jnp.bfloat16)
        stored.append((stream, tap_rows, pre_act, squashed))
        stream = next_stream

    def unit_back(unit_idx, grad_y):
        dilation = 3**unit_idx
        stream_in, tap_rows, pre_act, squashed = stored[unit_idx]
        grad_b = lax.dot_general(
            grad_y,
            weights_b[unit_idx],
            (((1,), (1,)), ((), ())),
            preferred_element_type=jnp.float32,
        )
        gate = (grad_b * elu_slope(pre_act)).astype(jnp.bfloat16)
        back_rows = jnp.concatenate(
            [shifted_rows(gate, -(tap_no - half) * dilation) for tap_no in range(KERNEL)],
            axis=1,
        )
        turned = jnp.transpose(weights_a[unit_idx], (0, 2, 1)).reshape(KERNEL * inner, channels)
        back = jnp.dot(back_rows, turned, preferred_element_type=jnp.float32)
        grad_next = (
            grad_y.astype(jnp.float32) + back * elu_slope(stream_in.astype(jnp.float32))
        ).astype(jnp.bfloat16)
        return (gate, grad_next)

    first_gates = [None] * UNITS
    first_grads = [None] * (UNITS + 1)
    grad_y = grad_top
    first_grads[UNITS] = grad_y
    for unit_idx in reversed(range(UNITS)):
        gate, grad_y = unit_back(unit_idx, grad_y)
        first_gates[unit_idx] = gate
        first_grads[unit_idx] = grad_y
    latent = lax.ppermute(grad_y, "segment", [(1, 0)])
    grads_a = [None] * UNITS
    grads_bias = [None] * UNITS
    grads_b = [None] * UNITS
    contract = (((0,), (0,)), ((), ()))
    grad_y = latent
    for unit_idx in reversed(range(UNITS)):
        stream_in, tap_rows, pre_act, squashed = stored[unit_idx]
        gate_two, grad_next = unit_back(unit_idx, grad_y)
        gate = jnp.where(is_decoder, first_gates[unit_idx][own], gate_two[own])
        grad_out = jnp.where(is_decoder, first_grads[unit_idx + 1][own], grad_y[own])
        unit_b = lax.dot_general(
            squashed[own], grad_out, contract, preferred_element_type=jnp.float32
        )
        unit_bias = jnp.sum(gate.astype(jnp.float32), axis=0)
        unit_a = lax.dot_general(
            tap_rows[own], gate, contract, preferred_element_type=jnp.float32
        ).reshape(KERNEL, channels, inner)
        grads_a[unit_idx] = unit_a
        grads_bias[unit_idx] = unit_bias
        grads_b[unit_idx] = unit_b
        grad_y = grad_next
    section_grad = jnp.where(is_decoder, first_grads[0][own], grad_y[own])
    rows_a = UNITS * KERNEL * channels
    rows_b = UNITS * inner
    flat_a = jnp.stack(grads_a).reshape(rows_a, inner)
    flat_b = jnp.concatenate(
        [
            jnp.stack(grads_b).reshape(rows_b, channels),
            jnp.pad(jnp.stack(grads_bias), ((0, 8 - UNITS), (0, 0))),
        ],
        axis=0,
    )
    flat_a, flat_b = lax.psum((flat_a, flat_b), ("dp", "seq"))
    total_a = flat_a.reshape(UNITS, KERNEL, channels, inner)
    total_b = flat_b[:rows_b].reshape(UNITS, inner, channels)
    total_bias = flat_b[rows_b : rows_b + UNITS]
    return (section_grad[None, None], total_a[None], total_bias[None], total_b[None])


def solution(mesh):
    placed = (
        P("segment", "dp", "seq", None),
        P("dp", "seq", None),
        P("dp", None),
        P("segment", None, None, None, None),
        P("segment", None, None),
        P("segment", None, None, None),
    )
    return jax.shard_map(
        shards,
        mesh=mesh,
        in_specs=placed,
        out_specs=(
            P("segment", "dp", "seq", None),
            P("segment", None, None, None, None),
            P("segment", None, None),
            P("segment", None, None, None),
        ),
        check_vma=False,
    )
```

```python
import jax
import jax.numpy as jnp
from jax import lax
from jax.sharding import PartitionSpec as P

KERNEL = 7
UNITS = 3


def with_halo(cells, sides, width):
    for axis, dim in sides:
        count = lax.axis_size(axis)
        ends = count - 1
        head = lax.slice_in_dim(cells, 0, width, axis=dim)
        tail = lax.slice_in_dim(cells, cells.shape[dim] - width, cells.shape[dim], axis=dim)
        cells = jnp.concatenate(
            [
                lax.ppermute(tail, axis, [(i, (i + 1) % count) for i in range(ends)]),
                cells,
                lax.ppermute(head, axis, [((i + 1) % count, i) for i in range(ends)]),
            ],
            axis=dim,
        )
    return cells


def spread(value, axis, root):
    mine = lax.axis_index(axis) == root
    return lax.psum(jnp.where(mine, value, jnp.zeros_like(value)), axis)


def elu_act(value):
    return jnp.where(value > 0, value, jnp.expm1(jnp.minimum(value, 0.0)))


def elu_slope(value):
    return jnp.where(value > 0, 1.0, jnp.exp(jnp.minimum(value, 0.0)))


def spread_acts(active, reach):
    return with_halo(active, (("seq", 0),), reach)


def spread_grads(gate, reach):
    return with_halo(gate, (("seq", 0),), reach)


def shards(saved_input, upstream, clip_lengths, conv_a, bias_a, conv_b):
    lengths = clip_lengths[0]
    weights_a = conv_a[0]
    biases_a = bias_a[0]
    weights_b = conv_b[0]
    frames = saved_input.shape[2]
    channels = saved_input.shape[3]
    inner = weights_a.shape[3]
    half = KERNEL // 2
    reaches = [half * 3**unit_idx for unit_idx in range(UNITS)]
    margin = -(-3 * sum(reaches) // 8) * 8
    window = -(-(sum(reaches) + 1) // 8) * 8
    span = frames + 2 * margin
    total = frames * lax.axis_size("seq")
    offset = lax.axis_index("seq") * frames
    is_decoder = lax.axis_index("segment") == 1
    clip_ends = jnp.cumsum(lengths)
    places = offset - margin + jnp.arange(span, dtype=jnp.int32)
    clip_of = jnp.sum((places[:, None] >= clip_ends[None, :]).astype(jnp.int32), axis=1)
    clip_of = jnp.where(places < 0, -1, clip_of)
    clip_of = jnp.where(places >= total, lengths.shape[0], clip_of)
    own = slice(margin, margin + frames)

    def linked(shift_by, ids):
        edge = abs(shift_by)
        rows = ids.shape[0]
        padded_ids = jnp.pad(ids, (edge, edge), constant_values=-2)
        return (padded_ids[edge + shift_by : edge + shift_by + rows] == ids)[:, None]

    def shifted_rows(values, shift_by, ids=clip_of):
        edge = abs(shift_by)
        rows = values.shape[0]
        padded = jnp.pad(values, ((edge, edge), (0, 0)))
        return jnp.where(
            linked(shift_by, ids),
            padded[edge + shift_by : edge + shift_by + rows],
            jnp.zeros((), values.dtype),
        )

    both = with_halo(
        jnp.concatenate([saved_input[0, 0], upstream[0]], axis=1), (("seq", 0),), margin
    )
    stream = both[:, :channels]
    grad_top = both[:, channels:]

    stored = []
    for unit_idx in range(UNITS):
        dilation = 3**unit_idx
        active = elu_act(stream.astype(jnp.float32)).astype(jnp.bfloat16)
        tap_rows = jnp.concatenate(
            [shifted_rows(active, (tap_no - half) * dilation) for tap_no in range(KERNEL)],
            axis=1,
        )
        pre_act = biases_a[unit_idx][None, :] + jnp.dot(
            tap_rows,
            weights_a[unit_idx].reshape(KERNEL * channels, inner),
            preferred_element_type=jnp.float32,
        )
        squashed = elu_act(pre_act).astype(jnp.bfloat16)
        next_stream = (
            stream.astype(jnp.float32)
            + jnp.dot(squashed, weights_b[unit_idx], preferred_element_type=jnp.float32)
        ).astype(jnp.bfloat16)
        stored.append((stream, tap_rows, pre_act, squashed))
        stream = next_stream

    def unit_back(unit_idx, grad_y, rows=slice(0, span)):
        dilation = 3**unit_idx
        stream_in, tap_rows, pre_act, squashed = stored[unit_idx]
        stream_in = stream_in[rows]
        pre_act = pre_act[rows]
        ids = clip_of[rows]
        grad_b = lax.dot_general(
            grad_y,
            weights_b[unit_idx],
            (((1,), (1,)), ((), ())),
            preferred_element_type=jnp.float32,
        )
        gate = (grad_b * elu_slope(pre_act)).astype(jnp.bfloat16)
        back_rows = jnp.concatenate(
            [shifted_rows(gate, -(tap_no - half) * dilation, ids) for tap_no in range(KERNEL)],
            axis=1,
        )
        turned = jnp.transpose(weights_a[unit_idx], (0, 2, 1)).reshape(KERNEL * inner, channels)
        back = jnp.dot(back_rows, turned, preferred_element_type=jnp.float32)
        grad_next = (
            grad_y.astype(jnp.float32) + back * elu_slope(stream_in.astype(jnp.float32))
        ).astype(jnp.bfloat16)
        return (gate, grad_next)

    first_gates = [None] * UNITS
    first_grads = [None] * (UNITS + 1)
    grad_y = grad_top
    first_grads[UNITS] = grad_y
    for unit_idx in reversed(range(UNITS)):
        gate, grad_y = unit_back(unit_idx, grad_y)
        first_gates[unit_idx] = gate
        first_grads[unit_idx] = grad_y
    latent = lax.ppermute(grad_y, "segment", [(1, 0)])
    grads_a = [None] * UNITS
    grads_bias = [None] * UNITS
    grads_b = [None] * UNITS
    contract = (((0,), (0,)), ((), ()))
    near = slice(margin - window, margin + frames + window)
    inside = slice(window, window + frames)
    grad_y = latent[near]
    for unit_idx in reversed(range(UNITS)):
        stream_in, tap_rows, pre_act, squashed = stored[unit_idx]
        gate_two, grad_next = unit_back(unit_idx, grad_y, near)
        gate = jnp.where(is_decoder, first_gates[unit_idx][own], gate_two[inside])
        grad_out = jnp.where(is_decoder, first_grads[unit_idx + 1][own], grad_y[inside])
        unit_b = lax.dot_general(
            squashed[own], grad_out, contract, preferred_element_type=jnp.float32
        )
        unit_bias = jnp.sum(gate.astype(jnp.float32), axis=0)
        unit_a = lax.dot_general(
            tap_rows[own], gate, contract, preferred_element_type=jnp.float32
        ).reshape(KERNEL, channels, inner)
        grads_a[unit_idx] = unit_a
        grads_bias[unit_idx] = unit_bias
        grads_b[unit_idx] = unit_b
        grad_y = grad_next
    section_grad = jnp.where(is_decoder, first_grads[0][own], grad_y[inside])
    rows_a = UNITS * KERNEL * channels
    rows_b = UNITS * inner
    flat_a = jnp.stack(grads_a).reshape(rows_a, inner)
    flat_b = jnp.concatenate(
        [
            jnp.stack(grads_b).reshape(rows_b, channels),
            jnp.pad(jnp.stack(grads_bias), ((0, 8 - UNITS), (0, 0))),
        ],
        axis=0,
    )
    flat_a, flat_b = lax.psum((flat_a, flat_b), ("dp", "seq"))
    total_a = flat_a.reshape(UNITS, KERNEL, channels, inner)
    total_b = flat_b[:rows_b].reshape(UNITS, inner, channels)
    total_bias = flat_b[rows_b : rows_b + UNITS]
    return (section_grad[None, None], total_a[None], total_bias[None], total_b[None])


def solution(mesh):
    placed = (
        P("segment", "dp", "seq", None),
        P("dp", "seq", None),
        P("dp", None),
        P("segment", None, None, None, None),
        P("segment", None, None),
        P("segment", None, None, None),
    )
    return jax.shard_map(
        shards,
        mesh=mesh,
        in_specs=placed,
        out_specs=(
            P("segment", "dp", "seq", None),
            P("segment", None, None, None, None),
            P("segment", None, None),
            P("segment", None, None, None),
        ),
        check_vma=False,
    )
```

```python
import jax
import jax.numpy as jnp
from jax import lax
from jax.sharding import PartitionSpec as P

KERNEL = 7
UNITS = 3


def with_halo(cells, sides, width):
    for axis, dim in sides:
        count = lax.axis_size(axis)
        ends = count - 1
        head = lax.slice_in_dim(cells, 0, width, axis=dim)
        tail = lax.slice_in_dim(cells, cells.shape[dim] - width, cells.shape[dim], axis=dim)
        cells = jnp.concatenate(
            [
                lax.ppermute(tail, axis, [(i, (i + 1) % count) for i in range(ends)]),
                cells,
                lax.ppermute(head, axis, [((i + 1) % count, i) for i in range(ends)]),
            ],
            axis=dim,
        )
    return cells


def spread(value, axis, root):
    mine = lax.axis_index(axis) == root
    return lax.psum(jnp.where(mine, value, jnp.zeros_like(value)), axis)


def elu_act(value):
    return jnp.where(value > 0, value, jnp.expm1(jnp.minimum(value, 0.0)))


def elu_slope(value):
    return jnp.where(value > 0, 1.0, jnp.exp(jnp.minimum(value, 0.0)))


def spread_acts(active, reach):
    return with_halo(active, (("seq", 0),), reach)


def spread_grads(gate, reach):
    return with_halo(gate, (("seq", 0),), reach)


def shards(saved_input, upstream, clip_lengths, conv_a, bias_a, conv_b):
    lengths = clip_lengths[0]
    weights_a = conv_a[0]
    biases_a = bias_a[0]
    weights_b = conv_b[0]
    frames = saved_input.shape[2]
    channels = saved_input.shape[3]
    inner = weights_a.shape[3]
    half = KERNEL // 2
    reaches = [half * 3**unit_idx for unit_idx in range(UNITS)]
    margin = -(-3 * sum(reaches) // 8) * 8
    window = -(-(sum(reaches) + 1) // 8) * 8
    reach_back = -(-(2 * sum(reaches) + 1) // 8) * 8
    span = frames + 2 * margin
    total = frames * lax.axis_size("seq")
    offset = lax.axis_index("seq") * frames
    is_decoder = lax.axis_index("segment") == 1
    clip_ends = jnp.cumsum(lengths)
    places = offset - margin + jnp.arange(span, dtype=jnp.int32)
    clip_of = jnp.sum((places[:, None] >= clip_ends[None, :]).astype(jnp.int32), axis=1)
    clip_of = jnp.where(places < 0, -1, clip_of)
    clip_of = jnp.where(places >= total, lengths.shape[0], clip_of)
    own = slice(margin, margin + frames)

    def linked(shift_by, ids):
        edge = abs(shift_by)
        rows = ids.shape[0]
        padded_ids = jnp.pad(ids, (edge, edge), constant_values=-2)
        return (padded_ids[edge + shift_by : edge + shift_by + rows] == ids)[:, None]

    def shifted_rows(values, shift_by, ids=clip_of):
        edge = abs(shift_by)
        rows = values.shape[0]
        padded = jnp.pad(values, ((edge, edge), (0, 0)))
        return jnp.where(
            linked(shift_by, ids),
            padded[edge + shift_by : edge + shift_by + rows],
            jnp.zeros((), values.dtype),
        )

    both = with_halo(
        jnp.concatenate([saved_input[0, 0], upstream[0]], axis=1), (("seq", 0),), margin
    )
    stream = both[:, :channels]
    grad_top = both[:, channels:]

    stored = []
    for unit_idx in range(UNITS):
        dilation = 3**unit_idx
        active = elu_act(stream.astype(jnp.float32)).astype(jnp.bfloat16)
        tap_rows = jnp.concatenate(
            [shifted_rows(active, (tap_no - half) * dilation) for tap_no in range(KERNEL)],
            axis=1,
        )
        pre_act = biases_a[unit_idx][None, :] + jnp.dot(
            tap_rows,
            weights_a[unit_idx].reshape(KERNEL * channels, inner),
            preferred_element_type=jnp.float32,
        )
        squashed = elu_act(pre_act).astype(jnp.bfloat16)
        next_stream = (
            stream.astype(jnp.float32)
            + jnp.dot(squashed, weights_b[unit_idx], preferred_element_type=jnp.float32)
        ).astype(jnp.bfloat16)
        stored.append((stream, tap_rows, pre_act, squashed))
        stream = next_stream

    def unit_back(unit_idx, grad_y, rows=slice(0, span)):
        dilation = 3**unit_idx
        stream_in, tap_rows, pre_act, squashed = stored[unit_idx]
        stream_in = stream_in[rows]
        pre_act = pre_act[rows]
        ids = clip_of[rows]
        grad_b = lax.dot_general(
            grad_y,
            weights_b[unit_idx],
            (((1,), (1,)), ((), ())),
            preferred_element_type=jnp.float32,
        )
        gate = (grad_b * elu_slope(pre_act)).astype(jnp.bfloat16)
        back_rows = jnp.concatenate(
            [shifted_rows(gate, -(tap_no - half) * dilation, ids) for tap_no in range(KERNEL)],
            axis=1,
        )
        turned = jnp.transpose(weights_a[unit_idx], (0, 2, 1)).reshape(KERNEL * inner, channels)
        back = jnp.dot(back_rows, turned, preferred_element_type=jnp.float32)
        grad_next = (
            grad_y.astype(jnp.float32) + back * elu_slope(stream_in.astype(jnp.float32))
        ).astype(jnp.bfloat16)
        return (gate, grad_next)

    first_gates = [None] * UNITS
    first_grads = [None] * (UNITS + 1)
    far = slice(margin - reach_back, margin + frames + reach_back)
    mine = slice(reach_back, reach_back + frames)
    grad_y = grad_top[far]
    first_grads[UNITS] = grad_y
    for unit_idx in reversed(range(UNITS)):
        gate, grad_y = unit_back(unit_idx, grad_y, far)
        first_gates[unit_idx] = gate
        first_grads[unit_idx] = grad_y
    latent = lax.ppermute(
        grad_y[reach_back - window : reach_back + frames + window], "segment", [(1, 0)]
    )
    grads_a = [None] * UNITS
    grads_bias = [None] * UNITS
    grads_b = [None] * UNITS
    contract = (((0,), (0,)), ((), ()))
    near = slice(margin - window, margin + frames + window)
    inside = slice(window, window + frames)
    grad_y = latent
    for unit_idx in reversed(range(UNITS)):
        stream_in, tap_rows, pre_act, squashed = stored[unit_idx]
        gate_two, grad_next = unit_back(unit_idx, grad_y, near)
        gate = jnp.where(is_decoder, first_gates[unit_idx][mine], gate_two[inside])
        grad_out = jnp.where(is_decoder, first_grads[unit_idx + 1][mine], grad_y[inside])
        unit_b = lax.dot_general(
            squashed[own], grad_out, contract, preferred_element_type=jnp.float32
        )
        unit_bias = jnp.sum(gate.astype(jnp.float32), axis=0)
        unit_a = lax.dot_general(
            tap_rows[own], gate, contract, preferred_element_type=jnp.float32
        ).reshape(KERNEL, channels, inner)
        grads_a[unit_idx] = unit_a
        grads_bias[unit_idx] = unit_bias
        grads_b[unit_idx] = unit_b
        grad_y = grad_next
    section_grad = jnp.where(is_decoder, first_grads[0][mine], grad_y[inside])
    rows_a = UNITS * KERNEL * channels
    rows_b = UNITS * inner
    flat_a = jnp.stack(grads_a).reshape(rows_a, inner)
    flat_b = jnp.concatenate(
        [
            jnp.stack(grads_b).reshape(rows_b, channels),
            jnp.pad(jnp.stack(grads_bias), ((0, 8 - UNITS), (0, 0))),
        ],
        axis=0,
    )
    flat_a, flat_b = lax.psum((flat_a, flat_b), ("dp", "seq"))
    total_a = flat_a.reshape(UNITS, KERNEL, channels, inner)
    total_b = flat_b[:rows_b].reshape(UNITS, inner, channels)
    total_bias = flat_b[rows_b : rows_b + UNITS]
    return (section_grad[None, None], total_a[None], total_bias[None], total_b[None])


def solution(mesh):
    placed = (
        P("segment", "dp", "seq", None),
        P("dp", "seq", None),
        P("dp", None),
        P("segment", None, None, None, None),
        P("segment", None, None),
        P("segment", None, None, None),
    )
    return jax.shard_map(
        shards,
        mesh=mesh,
        in_specs=placed,
        out_specs=(
            P("segment", "dp", "seq", None),
            P("segment", None, None, None, None),
            P("segment", None, None),
            P("segment", None, None, None),
        ),
        check_vma=False,
    )
```

```python
import jax
import jax.numpy as jnp
from jax import lax
from jax.sharding import PartitionSpec as P

KERNEL = 7
UNITS = 3


def with_halo(cells, sides, width):
    for axis, dim in sides:
        count = lax.axis_size(axis)
        ends = count - 1
        head = lax.slice_in_dim(cells, 0, width, axis=dim)
        tail = lax.slice_in_dim(cells, cells.shape[dim] - width, cells.shape[dim], axis=dim)
        cells = jnp.concatenate(
            [
                lax.ppermute(tail, axis, [(i, (i + 1) % count) for i in range(ends)]),
                cells,
                lax.ppermute(head, axis, [((i + 1) % count, i) for i in range(ends)]),
            ],
            axis=dim,
        )
    return cells


def spread(value, axis, root):
    mine = lax.axis_index(axis) == root
    return lax.psum(jnp.where(mine, value, jnp.zeros_like(value)), axis)


def elu_act(value):
    return jnp.where(value > 0, value, jnp.expm1(jnp.minimum(value, 0.0)))


def elu_slope(value):
    return jnp.where(value > 0, 1.0, jnp.exp(jnp.minimum(value, 0.0)))


def spread_acts(active, reach):
    return with_halo(active, (("seq", 0),), reach)


def spread_grads(gate, reach):
    return with_halo(gate, (("seq", 0),), reach)


def shards(saved_input, upstream, clip_lengths, conv_a, bias_a, conv_b):
    lengths = clip_lengths[0]
    weights_a = conv_a[0]
    biases_a = bias_a[0]
    weights_b = conv_b[0]
    frames = saved_input.shape[2]
    channels = saved_input.shape[3]
    inner = weights_a.shape[3]
    half = KERNEL // 2
    reaches = [half * 3**unit_idx for unit_idx in range(UNITS)]
    margin = -(-3 * sum(reaches) // 8) * 8
    window = -(-(sum(reaches) + 1) // 8) * 8
    span = frames + 2 * margin
    total = frames * lax.axis_size("seq")
    offset = lax.axis_index("seq") * frames
    is_decoder = lax.axis_index("segment") == 1
    clip_ends = jnp.cumsum(lengths)
    places = offset - margin + jnp.arange(span, dtype=jnp.int32)
    clip_of = jnp.sum((places[:, None] >= clip_ends[None, :]).astype(jnp.int32), axis=1)
    clip_of = jnp.where(places < 0, -1, clip_of)
    clip_of = jnp.where(places >= total, lengths.shape[0], clip_of)
    own = slice(margin, margin + frames)

    def linked(shift_by, ids):
        edge = abs(shift_by)
        rows = ids.shape[0]
        padded_ids = jnp.pad(ids, (edge, edge), constant_values=-2)
        return (padded_ids[edge + shift_by : edge + shift_by + rows] == ids)[:, None]

    def shifted_rows(values, shift_by, ids=clip_of):
        edge = abs(shift_by)
        rows = values.shape[0]
        padded = jnp.pad(values, ((edge, edge), (0, 0)))
        return jnp.where(
            linked(shift_by, ids),
            padded[edge + shift_by : edge + shift_by + rows],
            jnp.zeros((), values.dtype),
        )

    both = with_halo(
        jnp.concatenate([saved_input[0, 0], upstream[0]], axis=1), (("seq", 0),), margin
    )
    stream = both[:, :channels]
    grad_top = both[:, channels:]

    stored = []
    for unit_idx in range(UNITS):
        dilation = 3**unit_idx
        active = elu_act(stream.astype(jnp.float32)).astype(jnp.bfloat16)
        tap_rows = jnp.concatenate(
            [shifted_rows(active, (tap_no - half) * dilation) for tap_no in range(KERNEL)],
            axis=1,
        )
        pre_act = biases_a[unit_idx][None, :] + jnp.dot(
            tap_rows,
            weights_a[unit_idx].reshape(KERNEL * channels, inner),
            preferred_element_type=jnp.float32,
        )
        squashed = elu_act(pre_act).astype(jnp.bfloat16)
        next_stream = (
            stream.astype(jnp.float32)
            + jnp.dot(squashed, weights_b[unit_idx], preferred_element_type=jnp.float32)
        ).astype(jnp.bfloat16)
        stored.append((stream, tap_rows, pre_act, squashed))
        stream = next_stream

    def unit_back(unit_idx, grad_y, rows=slice(0, span)):
        dilation = 3**unit_idx
        stream_in, tap_rows, pre_act, squashed = stored[unit_idx]
        stream_in = stream_in[rows]
        pre_act = pre_act[rows]
        ids = clip_of[rows]
        grad_b = lax.dot_general(
            grad_y,
            weights_b[unit_idx],
            (((1,), (1,)), ((), ())),
            preferred_element_type=jnp.float32,
        )
        gate = (grad_b * elu_slope(pre_act)).astype(jnp.bfloat16)
        back = sum(
            lax.dot_general(
                shifted_rows(gate, -(tap_no - half) * dilation, ids),
                weights_a[unit_idx, tap_no],
                (((1,), (1,)), ((), ())),
                preferred_element_type=jnp.float32,
            )
            for tap_no in range(KERNEL)
        )
        grad_next = (
            grad_y.astype(jnp.float32) + back * elu_slope(stream_in.astype(jnp.float32))
        ).astype(jnp.bfloat16)
        return (gate, grad_next)

    first_gates = [None] * UNITS
    first_grads = [None] * (UNITS + 1)
    grad_y = grad_top
    first_grads[UNITS] = grad_y
    for unit_idx in reversed(range(UNITS)):
        gate, grad_y = unit_back(unit_idx, grad_y)
        first_gates[unit_idx] = gate
        first_grads[unit_idx] = grad_y
    latent = lax.ppermute(grad_y, "segment", [(1, 0)])
    grads_a = [None] * UNITS
    grads_bias = [None] * UNITS
    grads_b = [None] * UNITS
    contract = (((0,), (0,)), ((), ()))
    near = slice(margin - window, margin + frames + window)
    inside = slice(window, window + frames)
    grad_y = latent[near]
    for unit_idx in reversed(range(UNITS)):
        stream_in, tap_rows, pre_act, squashed = stored[unit_idx]
        gate_two, grad_next = unit_back(unit_idx, grad_y, near)
        gate = jnp.where(is_decoder, first_gates[unit_idx][own], gate_two[inside])
        grad_out = jnp.where(is_decoder, first_grads[unit_idx + 1][own], grad_y[inside])
        unit_b = lax.dot_general(
            squashed[own], grad_out, contract, preferred_element_type=jnp.float32
        )
        unit_bias = jnp.sum(gate.astype(jnp.float32), axis=0)
        unit_a = lax.dot_general(
            tap_rows[own], gate, contract, preferred_element_type=jnp.float32
        ).reshape(KERNEL, channels, inner)
        grads_a[unit_idx] = unit_a
        grads_bias[unit_idx] = unit_bias
        grads_b[unit_idx] = unit_b
        grad_y = grad_next
    section_grad = jnp.where(is_decoder, first_grads[0][own], grad_y[inside])
    rows_a = UNITS * KERNEL * channels
    rows_b = UNITS * inner
    flat_a = jnp.stack(grads_a).reshape(rows_a, inner)
    flat_b = jnp.concatenate(
        [
            jnp.stack(grads_b).reshape(rows_b, channels),
            jnp.pad(jnp.stack(grads_bias), ((0, 8 - UNITS), (0, 0))),
        ],
        axis=0,
    )
    flat_a, flat_b = lax.psum((flat_a, flat_b), ("dp", "seq"))
    total_a = flat_a.reshape(UNITS, KERNEL, channels, inner)
    total_b = flat_b[:rows_b].reshape(UNITS, inner, channels)
    total_bias = flat_b[rows_b : rows_b + UNITS]
    return (section_grad[None, None], total_a[None], total_bias[None], total_b[None])


def solution(mesh):
    placed = (
        P("segment", "dp", "seq", None),
        P("dp", "seq", None),
        P("dp", None),
        P("segment", None, None, None, None),
        P("segment", None, None),
        P("segment", None, None, None),
    )
    return jax.shard_map(
        shards,
        mesh=mesh,
        in_specs=placed,
        out_specs=(
            P("segment", "dp", "seq", None),
            P("segment", None, None, None, None),
            P("segment", None, None),
            P("segment", None, None, None),
        ),
        check_vma=False,
    )
```

```python
import jax
import jax.numpy as jnp
from jax import lax
from jax.sharding import PartitionSpec as P

KERNEL = 7
UNITS = 3


def with_halo(cells, sides, width):
    for axis, dim in sides:
        count = lax.axis_size(axis)
        ends = count - 1
        head = lax.slice_in_dim(cells, 0, width, axis=dim)
        tail = lax.slice_in_dim(cells, cells.shape[dim] - width, cells.shape[dim], axis=dim)
        cells = jnp.concatenate(
            [
                lax.ppermute(tail, axis, [(i, (i + 1) % count) for i in range(ends)]),
                cells,
                lax.ppermute(head, axis, [((i + 1) % count, i) for i in range(ends)]),
            ],
            axis=dim,
        )
    return cells


def spread(value, axis, root):
    mine = lax.axis_index(axis) == root
    return lax.psum(jnp.where(mine, value, jnp.zeros_like(value)), axis)


def elu_act(value):
    return jnp.where(value > 0, value, jnp.expm1(jnp.minimum(value, 0.0)))


def elu_slope(value):
    return jnp.where(value > 0, 1.0, jnp.exp(jnp.minimum(value, 0.0)))


def spread_acts(active, reach):
    return with_halo(active, (("seq", 0),), reach)


def spread_grads(gate, reach):
    return with_halo(gate, (("seq", 0),), reach)


def shards(saved_input, upstream, clip_lengths, conv_a, bias_a, conv_b):
    lengths = clip_lengths[0]
    weights_a = conv_a[0]
    biases_a = bias_a[0]
    weights_b = conv_b[0]
    frames = saved_input.shape[2]
    channels = saved_input.shape[3]
    inner = weights_a.shape[3]
    half = KERNEL // 2
    reaches = [half * 3**unit_idx for unit_idx in range(UNITS)]
    margin = -(-3 * sum(reaches) // 8) * 8
    window = -(-(sum(reaches) + 1) // 8) * 8
    span = frames + 2 * margin
    total = frames * lax.axis_size("seq")
    offset = lax.axis_index("seq") * frames
    is_decoder = lax.axis_index("segment") == 1
    clip_ends = jnp.cumsum(lengths)
    places = offset - margin + jnp.arange(span, dtype=jnp.int32)
    clip_of = jnp.sum((places[:, None] >= clip_ends[None, :]).astype(jnp.int32), axis=1)
    clip_of = jnp.where(places < 0, -1, clip_of)
    clip_of = jnp.where(places >= total, lengths.shape[0], clip_of)
    own = slice(margin, margin + frames)

    def linked(shift_by, ids):
        edge = abs(shift_by)
        rows = ids.shape[0]
        padded_ids = jnp.pad(ids, (edge, edge), constant_values=-2)
        return (padded_ids[edge + shift_by : edge + shift_by + rows] == ids)[:, None]

    def shifted_rows(values, shift_by, ids=clip_of):
        edge = abs(shift_by)
        rows = values.shape[0]
        padded = jnp.pad(values, ((edge, edge), (0, 0)))
        return jnp.where(
            linked(shift_by, ids),
            padded[edge + shift_by : edge + shift_by + rows],
            jnp.zeros((), values.dtype),
        )

    both = with_halo(
        jnp.concatenate([saved_input[0, 0], upstream[0]], axis=1), (("seq", 0),), margin
    )
    stream = both[:, :channels]
    grad_top = both[:, channels:]

    stored = []
    for unit_idx in range(UNITS):
        dilation = 3**unit_idx
        active = elu_act(stream.astype(jnp.float32)).astype(jnp.bfloat16)
        tap_rows = [
            shifted_rows(active, (tap_no - half) * dilation) for tap_no in range(KERNEL)
        ]
        pre_act = biases_a[unit_idx][None, :] + sum(
            jnp.dot(tap_rows[tap_no], weights_a[unit_idx, tap_no], preferred_element_type=jnp.float32)
            for tap_no in range(KERNEL)
        )
        squashed = elu_act(pre_act).astype(jnp.bfloat16)
        next_stream = (
            stream.astype(jnp.float32)
            + jnp.dot(squashed, weights_b[unit_idx], preferred_element_type=jnp.float32)
        ).astype(jnp.bfloat16)
        stored.append((stream, tap_rows, pre_act, squashed))
        stream = next_stream

    def unit_back(unit_idx, grad_y, rows=slice(0, span)):
        dilation = 3**unit_idx
        stream_in, tap_rows, pre_act, squashed = stored[unit_idx]
        stream_in = stream_in[rows]
        pre_act = pre_act[rows]
        ids = clip_of[rows]
        grad_b = lax.dot_general(
            grad_y,
            weights_b[unit_idx],
            (((1,), (1,)), ((), ())),
            preferred_element_type=jnp.float32,
        )
        gate = (grad_b * elu_slope(pre_act)).astype(jnp.bfloat16)
        back = sum(
            lax.dot_general(
                shifted_rows(gate, -(tap_no - half) * dilation, ids),
                weights_a[unit_idx, tap_no],
                (((1,), (1,)), ((), ())),
                preferred_element_type=jnp.float32,
            )
            for tap_no in range(KERNEL)
        )
        grad_next = (
            grad_y.astype(jnp.float32) + back * elu_slope(stream_in.astype(jnp.float32))
        ).astype(jnp.bfloat16)
        return (gate, grad_next)

    first_gates = [None] * UNITS
    first_grads = [None] * (UNITS + 1)
    grad_y = grad_top
    first_grads[UNITS] = grad_y
    for unit_idx in reversed(range(UNITS)):
        gate, grad_y = unit_back(unit_idx, grad_y)
        first_gates[unit_idx] = gate
        first_grads[unit_idx] = grad_y
    latent = lax.ppermute(grad_y, "segment", [(1, 0)])
    grads_a = [None] * UNITS
    grads_bias = [None] * UNITS
    grads_b = [None] * UNITS
    contract = (((0,), (0,)), ((), ()))
    near = slice(margin - window, margin + frames + window)
    inside = slice(window, window + frames)
    grad_y = latent[near]
    for unit_idx in reversed(range(UNITS)):
        stream_in, tap_rows, pre_act, squashed = stored[unit_idx]
        gate_two, grad_next = unit_back(unit_idx, grad_y, near)
        gate = jnp.where(is_decoder, first_gates[unit_idx][own], gate_two[inside])
        grad_out = jnp.where(is_decoder, first_grads[unit_idx + 1][own], grad_y[inside])
        unit_b = lax.dot_general(
            squashed[own], grad_out, contract, preferred_element_type=jnp.float32
        )
        unit_bias = jnp.sum(gate.astype(jnp.float32), axis=0)
        unit_a = jnp.stack(
            [
                lax.dot_general(rows[own], gate, contract, preferred_element_type=jnp.float32)
                for rows in tap_rows
            ]
        )
        grads_a[unit_idx] = unit_a
        grads_bias[unit_idx] = unit_bias
        grads_b[unit_idx] = unit_b
        grad_y = grad_next
    section_grad = jnp.where(is_decoder, first_grads[0][own], grad_y[inside])
    rows_a = UNITS * KERNEL * channels
    rows_b = UNITS * inner
    flat_a = jnp.stack(grads_a).reshape(rows_a, inner)
    flat_b = jnp.concatenate(
        [
            jnp.stack(grads_b).reshape(rows_b, channels),
            jnp.pad(jnp.stack(grads_bias), ((0, 8 - UNITS), (0, 0))),
        ],
        axis=0,
    )
    flat_a, flat_b = lax.psum((flat_a, flat_b), ("dp", "seq"))
    total_a = flat_a.reshape(UNITS, KERNEL, channels, inner)
    total_b = flat_b[:rows_b].reshape(UNITS, inner, channels)
    total_bias = flat_b[rows_b : rows_b + UNITS]
    return (section_grad[None, None], total_a[None], total_bias[None], total_b[None])


def solution(mesh):
    placed = (
        P("segment", "dp", "seq", None),
        P("dp", "seq", None),
        P("dp", None),
        P("segment", None, None, None, None),
        P("segment", None, None),
        P("segment", None, None, None),
    )
    return jax.shard_map(
        shards,
        mesh=mesh,
        in_specs=placed,
        out_specs=(
            P("segment", "dp", "seq", None),
            P("segment", None, None, None, None),
            P("segment", None, None),
            P("segment", None, None, None),
        ),
        check_vma=False,
    )
```
